128 devices in a mesh: grp: 4 (over y), tile: 32 (over x, z, core).
Axes of the slice: x: 4, y: 4, z: 4, core: 2. Of those that a mesh axis runs over, the one named last changes fastest.
Arguments:
- amp_tiles: bfloat16 [65536, 64, 64], P(('grp', 'tile')), may hold values from -6 to 6
- amp_row: int32 [65536], P(('grp', 'tile')), may hold values from 0 to 1024, as said below
- amp_col: int32 [65536], P(('grp', 'tile')), may hold values from 0 to 61
- cycle_panel: bfloat16 [3968, 3968], P('grp'), may hold values from -0.09375 to 0.09375
Outputs:
- residual: bfloat16 [65536, 64, 64], P(('grp', 'tile'))
The draws below stay inside these ranges and needn't reach their ends.
Inputs may be any that keep to these rules, and one draw needn't show every extreme that they name: `amp_row`: tiles n of block k = n // 512 lie in group h = k // 32: their rows are h * 256 to (h + 1) * 256 - 1, or 1024 for an empty slot. No two non-empty tiles name the same row and column tile. Within one block of 512 tiles at most 16 name rows of one run r * 8 to (r + 1) * 8 - 1, and 16 is reached in every draw; in every group some run has all its 496 tiles present.
All inputs are finite; a program needn't handle non-finite values.
Results may differ from the reference program's by a relative error of at most 0.001.
Values may be sent and summed in bfloat16 or wider, within the bound.
No kernel may reach another device: no remote copies, remote signals or barrier semaphores. Data moves between devices by JAX's collectives and lax.ppermute only.
A program may use at most 192 MiB of HBM per device.

```python
import jax
import jax.numpy as jnp
from jax import lax

TB = 64
NVT = 62
ROWT_DEV = 8
NV = 3968
NRG = 256
ROWS = 1024
CAP = 16
TPD = 512
TILES = 65536
N_GRP = 4
N_TILE = 32


def layout(key):
    base = jax.random.fold_in(key, 11)
    k_off, k_lev, k_coin, k_full, k_perm = jax.random.split(base, 5)
    blocks = ROWT_DEV * NVT
    offset = jax.random.randint(k_off, (N_GRP, N_TILE), 0, N_TILE)
    level = jax.random.randint(k_lev, (N_GRP, N_TILE, ROWT_DEV), 1, 9)
    coin = jax.random.randint(k_coin, (N_GRP, N_TILE, blocks), 0, 8)
    filled = jax.random.randint(k_full, (N_GRP,), 0, N_TILE)
    index_b = jnp.arange(blocks)
    level_b = level[:, :, index_b // NVT]
    dest_ids = jnp.arange(N_TILE)
    live = (coin < level_b) | (dest_ids[None, :, None] == filled[:, None, None])
    source = jnp.arange(N_TILE)[None, :, None, None]
    target = jnp.arange(N_TILE)[None, None, :, None]
    slot = jnp.arange(CAP)[None, None, None, :]
    group_ids = jnp.arange(N_GRP)[:, None, None, None]
    shifted = (source - offset[:, None, :, None]) % N_TILE
    block = slot * N_TILE + shifted
    inside = block < blocks
    safe = jnp.minimum(block, blocks - 1)
    live_here = live[group_ids, target, safe]
    valid = inside & live_here
    rows = jnp.where(valid, group_ids * NRG + target * ROWT_DEV + safe // NVT, ROWS)
    cols = safe % NVT
    rows = rows.reshape(N_GRP * N_TILE, TPD)
    cols = cols.reshape(N_GRP * N_TILE, TPD)
    keys = jax.random.split(k_perm, N_GRP * N_TILE)
    order = jax.vmap(lambda sub: jax.random.permutation(sub, TPD))(keys)
    rows = jnp.take_along_axis(rows, order, axis=1)
    cols = jnp.take_along_axis(cols, order, axis=1)
    return (rows.reshape(-1).astype(jnp.int32), cols.reshape(-1).astype(jnp.int32))


def draw_amp_row(key, part):
    return layout(key)[0]


def draw_amp_col(key, part):
    return layout(key)[1]


def shard_levels(stream_key, dims, cuts, smallest, largest):
    def one(axis_at, shards_of):
        heights = jax.random.uniform(jax.random.fold_in(jax.random.fold_in(stream_key, 6), axis_at), (shards_of,), jnp.float32, smallest / len(cuts), largest / len(cuts))
        return jnp.repeat(jnp.exp(heights), dims[axis_at] // shards_of).reshape((-1,) + (1,) * (len(dims) - axis_at - 1))

    level = one(*cuts[0])
    for cut in cuts[1:]:
        level = level * one(*cut)
    return level


def scatter_about(own_key, extent, spread, limit, cuts=(), kind=jnp.bfloat16):
    values = spread * jax.random.normal(own_key, extent, jnp.float32)
    if cuts:
        values = values * shard_levels(own_key, extent, cuts, -0.22, 0.18)
    return jnp.clip(values, -limit, limit).astype(kind)


def setup_inputs(seed: int = 0) -> dict:
    key_list = jax.random.split(jax.random.key(seed), 5)
    amp_tiles = scatter_about(key_list[0], (TILES, TB, TB), 1.0, 6.0, ((0, 128),))
    amp_row = draw_amp_row(jax.random.fold_in(key_list[4], 71), 0)
    amp_col = draw_amp_col(jax.random.fold_in(key_list[4], 71), 0)
    cycle_panel = scatter_about(key_list[3], (NV, NV), NV ** -0.5, 0.09375, ((0, 4),))
    return dict(amp_tiles=amp_tiles, amp_row=amp_row, amp_col=amp_col, cycle_panel=cycle_panel)


def reference(amp_tiles, amp_row, amp_col, cycle_panel):
    tiles = amp_tiles.reshape(N_GRP, N_TILE * TPD, TB * TB)
    rows = amp_row.reshape(N_GRP, N_TILE * TPD)
    cols = amp_col.reshape(N_GRP, N_TILE * TPD)

    def one_group(items):
        group, group_tiles, group_rows, group_cols = items
        local = group_rows - group * NRG
        live = local < NRG
        block = jnp.where(live, local * NVT + group_cols, NRG * NVT).astype(jnp.int32)
        dense = jnp.zeros((NRG * NVT, TB * TB), jnp.bfloat16).at[block].set(group_tiles, mode="drop")
        dense = dense.reshape(NRG, NVT, TB, TB).transpose(0, 2, 1, 3).reshape(NRG * TB, NVT * TB)
        cycle = jnp.dot(dense, cycle_panel, preferred_element_type=jnp.float32).astype(jnp.bfloat16)
        blocks = cycle.reshape(NRG, TB, NVT, TB).transpose(0, 2, 1, 3).reshape(NRG * NVT, TB * TB)
        return jnp.take(blocks, block, axis=0, mode="fill", fill_value=0)

    result = lax.map(one_group, (jnp.arange(N_GRP, dtype=jnp.int32), tiles, rows, cols))
    return result.reshape(TILES, TB, TB)
```

```python
import jax
import jax.numpy as jnp
from jax import lax
from jax.sharding import PartitionSpec as P

ROWT_DEV = 8


def layer(amp_tiles, amp_row, amp_col, cycle_panel):
    parts = lax.axis_size("tile")
    count = amp_tiles.shape[0]
    capacity = count // parts
    edge = amp_tiles.shape[1]
    width = cycle_panel.shape[1]
    nvt = width // edge
    per_dest = ROWT_DEV * nvt
    group_rows = ROWT_DEV * parts
    first = lax.axis_index("grp") * group_rows
    local_row = amp_row - first
    live = local_row < group_rows
    target = jnp.where(live, local_row // ROWT_DEV, parts)
    onehot = (target[:, None] == jnp.arange(parts)[None, :]).astype(jnp.int32)
    rank = jnp.sum(jnp.cumsum(onehot, axis=0) * onehot, axis=1) - 1
    position = jnp.where(live, target * capacity + rank, parts * capacity)
    block_id = local_row % ROWT_DEV * nvt + amp_col
    flat = amp_tiles.reshape(count, edge * edge)
    send_tiles = (
        jnp.zeros((parts * capacity, edge * edge), jnp.bfloat16).at[position].set(flat, mode="drop")
    )
    send_ids = (
        jnp.full((parts * capacity,), per_dest, jnp.int32).at[position].set(block_id, mode="drop")
    )
    recv_tiles, recv_ids = (
        lax.all_to_all(send_tiles, "tile", split_axis=0, concat_axis=0, tiled=True),
        lax.all_to_all(send_ids, "tile", split_axis=0, concat_axis=0, tiled=True),
    )
    dense = (
        jnp.zeros((per_dest, edge * edge), jnp.bfloat16).at[recv_ids].set(recv_tiles, mode="drop")
    )
    dense = (
        dense.reshape(ROWT_DEV, nvt, edge, edge)
        .transpose(0, 2, 1, 3)
        .reshape(ROWT_DEV * edge, width)
    )
    core = lax.axis_index("tile") % 2
    span = (width // 2 + 127) // 128 * 128
    mine = lax.dynamic_slice_in_dim(cycle_panel, core * (width - span), span, axis=1)
    gathered = lax.all_gather(mine, "grp", axis=0, tiled=True)
    partner = lax.ppermute(gathered, "tile", [(i, i ^ 1) for i in range(parts)])
    out_mine = jnp.dot(dense, gathered, preferred_element_type=jnp.float32).astype(jnp.bfloat16)
    out_partner = jnp.dot(dense, partner, preferred_element_type=jnp.float32).astype(jnp.bfloat16)
    cycle = jnp.zeros((ROWT_DEV * edge, width), jnp.bfloat16)
    cycle = lax.dynamic_update_slice_in_dim(cycle, out_partner, (1 - core) * (width - span), axis=1)
    cycle = lax.dynamic_update_slice_in_dim(cycle, out_mine, core * (width - span), axis=1)
    blocks_out = (
        cycle.reshape(ROWT_DEV, edge, nvt, edge)
        .transpose(0, 2, 1, 3)
        .reshape(per_dest, edge * edge)
    )
    answer = jnp.take(blocks_out, recv_ids, axis=0, mode="fill", fill_value=0)
    returned = lax.all_to_all(answer, "tile", split_axis=0, concat_axis=0, tiled=True)
    result = jnp.take(returned, position, axis=0, mode="fill", fill_value=0)
    return result.reshape(count, edge, edge)


def solution(mesh):
    in_specs = (
        P(("grp", "tile"), None, None),
        P(("grp", "tile")),
        P(("grp", "tile")),
        P("grp", None),
    )
    out_specs = P(("grp", "tile"), None, None)
    return jax.shard_map(layer, mesh=mesh, in_specs=in_specs, out_specs=out_specs, check_vma=False)
```

```python
import jax
import jax.numpy as jnp
from jax import lax
from jax.sharding import PartitionSpec as P

ROWT_DEV = 8


def pick_rows(index, count, data):
    onehot = (index[None, :] == jnp.arange(count)[:, None]).astype(data.dtype)
    return jnp.dot(onehot, data, preferred_element_type=jnp.float32).astype(data.dtype)


def take_rows(index, data):
    onehot = (index[:, None] == jnp.arange(data.shape[0])[None, :]).astype(data.dtype)
    return jnp.dot(onehot, data, preferred_element_type=jnp.float32).astype(data.dtype)


def to_blocks(out, edge):
    rows, cols = out.shape
    return (
        out.reshape(rows // edge, edge, cols // edge, edge)
        .transpose(0, 2, 1, 3)
        .reshape(rows // edge * (cols // edge), edge * edge)
    )


def layer(amp_tiles, amp_row, amp_col, cycle_panel):
    parts = lax.axis_size("tile")
    count = amp_tiles.shape[0]
    capacity = count // parts
    edge = amp_tiles.shape[1]
    width = cycle_panel.shape[1]
    nvt = width // edge
    per_dest = ROWT_DEV * nvt
    group_rows = ROWT_DEV * parts
    first = lax.axis_index("grp") * group_rows
    local_row = amp_row - first
    live = local_row < group_rows
    target = jnp.where(live, local_row // ROWT_DEV, parts)
    onehot = (target[:, None] == jnp.arange(parts)[None, :]).astype(jnp.int32)
    rank = jnp.sum(jnp.cumsum(onehot, axis=0) * onehot, axis=1) - 1
    position = jnp.where(live, target * capacity + rank, parts * capacity)
    block_id = local_row % ROWT_DEV * nvt + amp_col
    flat = amp_tiles.reshape(count, edge * edge)
    send_tiles = pick_rows(position, parts * capacity, flat)
    send_ids = (
        jnp.full((parts * capacity,), per_dest, jnp.int32).at[position].set(block_id, mode="drop")
    )
    recv_tiles, recv_ids = (
        lax.all_to_all(send_tiles, "tile", split_axis=0, concat_axis=0, tiled=True),
        lax.all_to_all(send_ids, "tile", split_axis=0, concat_axis=0, tiled=True),
    )
    dense = pick_rows(recv_ids, per_dest, recv_tiles)
    dense = (
        dense.reshape(ROWT_DEV, nvt, edge, edge)
        .transpose(0, 2, 1, 3)
        .reshape(ROWT_DEV * edge, width)
    )
    core = lax.axis_index("tile") % 2
    span = (width // 2 + 127) // 128 * 128
    shift = (width - span) // edge
    mine = lax.dynamic_slice_in_dim(cycle_panel, core * (width - span), span, axis=1)
    gathered = lax.all_gather(mine, "grp", axis=0, tiled=True)
    partner = lax.ppermute(gathered, "tile", [(i, i ^ 1) for i in range(parts)])
    half = span // edge
    valid = recv_ids < per_dest
    row_t = recv_ids // nvt
    col_t = recv_ids % nvt
    col_mine = col_t - core * shift
    in_mine = valid & (col_mine >= 0) & (col_mine < half)
    col_partner = col_t - (1 - core) * shift
    in_partner = valid & ~in_mine
    idx_mine = jnp.where(in_mine, row_t * half + col_mine, ROWT_DEV * half)
    idx_partner = jnp.where(in_partner, row_t * half + col_partner, ROWT_DEV * half)
    out_mine = jnp.dot(dense, gathered, preferred_element_type=jnp.float32).astype(jnp.bfloat16)
    ans_mine = take_rows(idx_mine, to_blocks(out_mine, edge))
    out_partner = jnp.dot(dense, partner, preferred_element_type=jnp.float32).astype(jnp.bfloat16)
    ans_partner = take_rows(idx_partner, to_blocks(out_partner, edge))
    answer = ans_mine + ans_partner
    returned = lax.all_to_all(answer, "tile", split_axis=0, concat_axis=0, tiled=True)
    onehot_back = (position[None, :] == jnp.arange(parts * capacity)[:, None]).astype(returned.dtype)
    result_t = jnp.dot(returned.T, onehot_back, preferred_element_type=jnp.float32).astype(returned.dtype)
    return result_t.T.reshape(count, edge, edge)


def solution(mesh):
    in_specs = (
        P(("grp", "tile"), None, None),
        P(("grp", "tile")),
        P(("grp", "tile")),
        P("grp", None),
    )
    out_specs = P(("grp", "tile"), None, None)
    return jax.shard_map(layer, mesh=mesh, in_specs=in_specs, out_specs=out_specs, check_vma=False)
```

```python
import jax
import jax.numpy as jnp
from jax import lax
from jax.sharding import PartitionSpec as P
from jax.experimental import pallas as pl
from jax.experimental.pallas import tpu as pltpu

ROWT_DEV = 8
CHUNKS = 4


def pick_rows(index, count, data):
    onehot = (index[None, :] == jnp.arange(count)[:, None]).astype(data.dtype)
    return jnp.dot(onehot, data, preferred_element_type=jnp.float32).astype(data.dtype)


def take_rows(index, data):
    onehot = (index[:, None] == jnp.arange(data.shape[0])[None, :]).astype(data.dtype)
    return jnp.dot(onehot, data, preferred_element_type=jnp.float32).astype(data.dtype)


def tiles_to_rows(tiles, row_tiles, edge):
    col_tiles = tiles.shape[0] // row_tiles

    def kernel(x_ref, o_ref):
        for r in range(row_tiles):
            x = x_ref[r * col_tiles : (r + 1) * col_tiles, :]
            x = jnp.swapaxes(x.reshape(col_tiles, edge, edge), 0, 1)
            o_ref[r * edge : (r + 1) * edge, :] = x.reshape(edge, col_tiles * edge)

    nbytes = tiles.size * tiles.dtype.itemsize
    return pl.pallas_call(
        kernel,
        out_shape=jax.ShapeDtypeStruct((row_tiles * edge, col_tiles * edge), tiles.dtype),
        in_specs=[pl.BlockSpec(memory_space=pltpu.VMEM)],
        out_specs=pl.BlockSpec(memory_space=pltpu.VMEM),
        cost_estimate=pl.CostEstimate(flops=0, transcendentals=0, bytes_accessed=2 * nbytes),
    )(tiles)


def rows_to_tiles(rows, edge):
    row_tiles = rows.shape[0] // edge
    col_tiles = rows.shape[1] // edge

    def kernel(x_ref, o_ref):
        for r in range(row_tiles):
            x = x_ref[r * edge : (r + 1) * edge, :]
            x = jnp.swapaxes(x.reshape(edge, col_tiles, edge), 0, 1)
            o_ref[r * col_tiles : (r + 1) * col_tiles, :] = x.reshape(col_tiles, edge * edge)

    nbytes = rows.size * rows.dtype.itemsize
    return pl.pallas_call(
        kernel,
        out_shape=jax.ShapeDtypeStruct((row_tiles * col_tiles, edge * edge), rows.dtype),
        in_specs=[pl.BlockSpec(memory_space=pltpu.VMEM)],
        out_specs=pl.BlockSpec(memory_space=pltpu.VMEM),
        cost_estimate=pl.CostEstimate(flops=0, transcendentals=0, bytes_accessed=2 * nbytes),
    )(rows)


def layer(amp_tiles, amp_row, amp_col, cycle_panel):
    parts = lax.axis_size("tile")
    count = amp_tiles.shape[0]
    capacity = count // parts
    edge = amp_tiles.shape[1]
    width = cycle_panel.shape[1]
    nvt = width // edge
    per_dest = ROWT_DEV * nvt
    group_rows = ROWT_DEV * parts
    first = lax.axis_index("grp") * group_rows
    local_row = amp_row - first
    live = local_row < group_rows
    target = jnp.where(live, local_row // ROWT_DEV, parts)
    onehot = (target[:, None] == jnp.arange(parts)[None, :]).astype(jnp.int32)
    rank = jnp.sum(jnp.cumsum(onehot, axis=0) * onehot, axis=1) - 1
    position = jnp.where(live, target * capacity + rank, parts * capacity)
    block_id = local_row % ROWT_DEV * nvt + amp_col
    flat = amp_tiles.reshape(count, edge * edge)
    send_tiles = pick_rows(position, parts * capacity, flat)
    send_ids = (
        jnp.full((parts * capacity,), per_dest, jnp.int32).at[position].set(block_id, mode="drop")
    )
    recv_tiles, recv_ids = (
        lax.all_to_all(send_tiles, "tile", split_axis=0, concat_axis=0, tiled=True),
        lax.all_to_all(send_ids, "tile", split_axis=0, concat_axis=0, tiled=True),
    )
    dense = tiles_to_rows(pick_rows(recv_ids, per_dest, recv_tiles), ROWT_DEV, edge)
    core = lax.axis_index("tile") % 2
    span = (width // 2 + 127) // 128 * 128
    shift = (width - span) // edge
    half = span // edge
    chunk = half // CHUNKS
    valid = recv_ids < per_dest
    row_t = recv_ids // nvt
    col_t = recv_ids % nvt
    col_mine = col_t - core * shift
    in_mine = valid & (col_mine >= 0) & (col_mine < half)
    col_partner = col_t - (1 - core) * shift
    in_partner = valid & ~in_mine
    unused = ROWT_DEV * chunk
    pieces = []
    for q in range(CHUNKS):
        mine = lax.dynamic_slice_in_dim(
            cycle_panel, core * (width - span) + q * chunk * edge, chunk * edge, axis=1
        )
        gathered = lax.all_gather(mine, "grp", axis=0, tiled=True)
        partner = lax.ppermute(gathered, "tile", [(i, i ^ 1) for i in range(parts)])
        lm = col_mine - q * chunk
        idx_mine = jnp.where(in_mine & (lm >= 0) & (lm < chunk), row_t * chunk + lm, unused)
        lp = col_partner - q * chunk
        idx_partner = jnp.where(in_partner & (lp >= 0) & (lp < chunk), row_t * chunk + lp, unused)
        out_mine = jnp.dot(dense, gathered, preferred_element_type=jnp.float32).astype(jnp.bfloat16)
        pieces.append(take_rows(idx_mine, rows_to_tiles(out_mine, edge)))
        out_partner = jnp.dot(dense, partner, preferred_element_type=jnp.float32).astype(jnp.bfloat16)
        pieces.append(take_rows(idx_partner, rows_to_tiles(out_partner, edge)))
    answer = pieces[0]
    for piece in pieces[1:]:
        answer = answer + piece
    returned = lax.all_to_all(answer, "tile", split_axis=0, concat_axis=0, tiled=True)
    onehot_back = (position[None, :] == jnp.arange(parts * capacity)[:, None]).astype(returned.dtype)
    result_t = jnp.dot(returned.T, onehot_back, preferred_element_type=jnp.float32).astype(returned.dtype)
    return result_t.T.reshape(count, edge, edge)


def solution(mesh):
    in_specs = (
        P(("grp", "tile"), None, None),
        P(("grp", "tile")),
        P(("grp", "tile")),
        P("grp", None),
    )
    out_specs = P(("grp", "tile"), None, None)
    return jax.shard_map(layer, mesh=mesh, in_specs=in_specs, out_specs=out_specs, check_vma=False)
```

```python
import jax
import jax.numpy as jnp
from jax import lax
from jax.sharding import PartitionSpec as P
from jax.experimental import pallas as pl
from jax.experimental.pallas import tpu as pltpu

ROWT_DEV = 8


def pick_rows(index, count, data):
    onehot = (index[None, :] == jnp.arange(count)[:, None]).astype(data.dtype)
    return jnp.dot(onehot, data, preferred_element_type=jnp.float32).astype(data.dtype)


def take_rows(index, data):
    onehot = (index[:, None] == jnp.arange(data.shape[0])[None, :]).astype(data.dtype)
    return jnp.dot(onehot, data, preferred_element_type=jnp.float32).astype(data.dtype)


def tiles_to_rows(tiles, row_tiles, edge):
    col_tiles = tiles.shape[0] // row_tiles

    def kernel(x_ref, o_ref):
        for r in range(row_tiles):
            x = x_ref[r * col_tiles : (r + 1) * col_tiles, :]
            x = jnp.swapaxes(x.reshape(col_tiles, edge, edge), 0, 1)
            o_ref[r * edge : (r + 1) * edge, :] = x.reshape(edge, col_tiles * edge)

    nbytes = tiles.size * tiles.dtype.itemsize
    return pl.pallas_call(
        kernel,
        out_shape=jax.ShapeDtypeStruct((row_tiles * edge, col_tiles * edge), tiles.dtype),
        in_specs=[pl.BlockSpec(memory_space=pltpu.VMEM)],
        out_specs=pl.BlockSpec(memory_space=pltpu.VMEM),
        cost_estimate=pl.CostEstimate(flops=0, transcendentals=0, bytes_accessed=2 * nbytes),
    )(tiles)


def rows_to_tiles(rows, edge):
    row_tiles = rows.shape[0] // edge
    col_tiles = rows.shape[1] // edge

    def kernel(x_ref, o_ref):
        for r in range(row_tiles):
            x = x_ref[r * edge : (r + 1) * edge, :]
            x = jnp.swapaxes(x.reshape(edge, col_tiles, edge), 0, 1)
            o_ref[r * col_tiles : (r + 1) * col_tiles, :] = x.reshape(col_tiles, edge * edge)

    nbytes = rows.size * rows.dtype.itemsize
    return pl.pallas_call(
        kernel,
        out_shape=jax.ShapeDtypeStruct((row_tiles * col_tiles, edge * edge), rows.dtype),
        in_specs=[pl.BlockSpec(memory_space=pltpu.VMEM)],
        out_specs=pl.BlockSpec(memory_space=pltpu.VMEM),
        cost_estimate=pl.CostEstimate(flops=0, transcendentals=0, bytes_accessed=2 * nbytes),
    )(rows)


def layer(amp_tiles, amp_row, amp_col, cycle_panel):
    parts = lax.axis_size("tile")
    count = amp_tiles.shape[0]
    capacity = count // parts
    edge = amp_tiles.shape[1]
    width = cycle_panel.shape[1]
    nvt = width // edge
    per_dest = ROWT_DEV * nvt
    group_rows = ROWT_DEV * parts
    first = lax.axis_index("grp") * group_rows
    local_row = amp_row - first
    live = local_row < group_rows
    target = jnp.where(live, local_row // ROWT_DEV, parts)
    onehot = (target[:, None] == jnp.arange(parts)[None, :]).astype(jnp.int32)
    rank = jnp.sum(jnp.cumsum(onehot, axis=0) * onehot, axis=1) - 1
    position = jnp.where(live, target * capacity + rank, parts * capacity)
    block_id = local_row % ROWT_DEV * nvt + amp_col
    flat = amp_tiles.reshape(count, edge * edge)
    send_tiles = pick_rows(position, parts * capacity, flat)
    send_ids = (
        jnp.full((parts * capacity,), per_dest, jnp.int32).at[position].set(block_id, mode="drop")
    )
    recv_tiles, recv_ids = (
        lax.all_to_all(send_tiles, "tile", split_axis=0, concat_axis=0, tiled=True),
        lax.all_to_all(send_ids, "tile", split_axis=0, concat_axis=0, tiled=True),
    )
    dense = tiles_to_rows(pick_rows(recv_ids, per_dest, recv_tiles), ROWT_DEV, edge)
    core = lax.axis_index("tile") % 2
    span = (width // 2 + 127) // 128 * 128
    shift = (width - span) // edge
    mine = lax.dynamic_slice_in_dim(cycle_panel, core * (width - span), span, axis=1)
    gathered = lax.all_gather(mine, "grp", axis=0, tiled=True)
    partner = lax.ppermute(gathered, "tile", [(i, i ^ 1) for i in range(parts)])
    half = span // edge
    valid = recv_ids < per_dest
    row_t = recv_ids // nvt
    col_t = recv_ids % nvt
    col_mine = col_t - core * shift
    in_mine = valid & (col_mine >= 0) & (col_mine < half)
    col_partner = col_t - (1 - core) * shift
    in_partner = valid & ~in_mine
    idx_mine = jnp.where(in_mine, row_t * half + col_mine, ROWT_DEV * half)
    idx_partner = jnp.where(in_partner, row_t * half + col_partner, ROWT_DEV * half)
    out_mine = jnp.dot(dense, gathered, preferred_element_type=jnp.float32).astype(jnp.bfloat16)
    ans_mine = take_rows(idx_mine, rows_to_tiles(out_mine, edge))
    out_partner = jnp.dot(dense, partner, preferred_element_type=jnp.float32).astype(jnp.bfloat16)
    ans_partner = take_rows(idx_partner, rows_to_tiles(out_partner, edge))
    answer = ans_mine + ans_partner
    returned = lax.all_to_all(answer, "tile", split_axis=0, concat_axis=0, tiled=True)
    onehot_back = (position[None, :] == jnp.arange(parts * capacity)[:, None]).astype(returned.dtype)
    result_t = jnp.dot(returned.T, onehot_back, preferred_element_type=jnp.float32).astype(returned.dtype)
    return result_t.T.reshape(count, edge, edge)


def solution(mesh):
    in_specs = (
        P(("grp", "tile"), None, None),
        P(("grp", "tile")),
        P(("grp", "tile")),
        P("grp", None),
    )
    out_specs = P(("grp", "tile"), None, None)
    return jax.shard_map(layer, mesh=mesh, in_specs=in_specs, out_specs=out_specs, check_vma=False)
```

```python
import jax
import jax.numpy as jnp
from jax import lax
from jax.sharding import PartitionSpec as P
from jax.experimental import pallas as pl
from jax.experimental.pallas import tpu as pltpu

ROWT_DEV = 8
PLANE = 4


def pick_rows(index, count, data):
    onehot = (index[None, :] == jnp.arange(count)[:, None]).astype(data.dtype)
    return jnp.dot(onehot, data, preferred_element_type=jnp.float32).astype(data.dtype)


def take_rows(index, data):
    onehot = (index[:, None] == jnp.arange(data.shape[0])[None, :]).astype(data.dtype)
    return jnp.dot(onehot, data, preferred_element_type=jnp.float32).astype(data.dtype)


def tiles_to_rows(tiles, row_tiles, edge):
    col_tiles = tiles.shape[0] // row_tiles

    def kernel(x_ref, o_ref):
        for r in range(row_tiles):
            x = x_ref[r * col_tiles : (r + 1) * col_tiles, :]
            x = jnp.swapaxes(x.reshape(col_tiles, edge, edge), 0, 1)
            o_ref[r * edge : (r + 1) * edge, :] = x.reshape(edge, col_tiles * edge)

    nbytes = tiles.size * tiles.dtype.itemsize
    return pl.pallas_call(
        kernel,
        out_shape=jax.ShapeDtypeStruct((row_tiles * edge, col_tiles * edge), tiles.dtype),
        in_specs=[pl.BlockSpec(memory_space=pltpu.VMEM)],
        out_specs=pl.BlockSpec(memory_space=pltpu.VMEM),
        cost_estimate=pl.CostEstimate(flops=0, transcendentals=0, bytes_accessed=2 * nbytes),
    )(tiles)


def rows_to_tiles(rows, edge):
    row_tiles = rows.shape[0] // edge
    col_tiles = rows.shape[1] // edge

    def kernel(x_ref, o_ref):
        for r in range(row_tiles):
            x = x_ref[r * edge : (r + 1) * edge, :]
            x = jnp.swapaxes(x.reshape(edge, col_tiles, edge), 0, 1)
            o_ref[r * col_tiles : (r + 1) * col_tiles, :] = x.reshape(col_tiles, edge * edge)

    nbytes = rows.size * rows.dtype.itemsize
    return pl.pallas_call(
        kernel,
        out_shape=jax.ShapeDtypeStruct((row_tiles * col_tiles, edge * edge), rows.dtype),
        in_specs=[pl.BlockSpec(memory_space=pltpu.VMEM)],
        out_specs=pl.BlockSpec(memory_space=pltpu.VMEM),
        cost_estimate=pl.CostEstimate(flops=0, transcendentals=0, bytes_accessed=2 * nbytes),
    )(rows)


def layer(amp_tiles, amp_row, amp_col, cycle_panel):
    parts = lax.axis_size("tile")
    count = amp_tiles.shape[0]
    capacity = count // parts
    edge = amp_tiles.shape[1]
    width = cycle_panel.shape[1]
    nvt = width // edge
    per_dest = ROWT_DEV * nvt
    group_rows = ROWT_DEV * parts
    first = lax.axis_index("grp") * group_rows
    local_row = amp_row - first
    live = local_row < group_rows
    target = jnp.where(live, local_row // ROWT_DEV, parts)
    onehot = (target[:, None] == jnp.arange(parts)[None, :]).astype(jnp.int32)
    rank = jnp.sum(jnp.cumsum(onehot, axis=0) * onehot, axis=1) - 1
    position = jnp.where(live, target * capacity + rank, parts * capacity)
    block_id = local_row % ROWT_DEV * nvt + amp_col
    flat = amp_tiles.reshape(count, edge * edge)
    send_tiles = pick_rows(position, parts * capacity, flat)
    send_ids = (
        jnp.full((parts * capacity,), per_dest, jnp.int32).at[position].set(block_id, mode="drop")
    )
    recv_tiles, recv_ids = (
        lax.all_to_all(send_tiles, "tile", split_axis=0, concat_axis=0, tiled=True),
        lax.all_to_all(send_ids, "tile", split_axis=0, concat_axis=0, tiled=True),
    )
    dense = tiles_to_rows(pick_rows(recv_ids, per_dest, recv_tiles), ROWT_DEV, edge)
    tile = lax.axis_index("tile")
    core = tile % 2
    chip = tile // 2
    side = PLANE
    cx = chip // side
    cz = chip % side
    colour = (cx + cz) % 2
    quarter = 1024
    nq = 4
    qt = quarter // edge
    base = [min(q * quarter, width - quarter) for q in range(nq)]
    mine_q = 2 * colour + core
    start_col = jnp.where(mine_q == nq - 1, base[nq - 1], mine_q * quarter)
    mine = lax.dynamic_slice_in_dim(cycle_panel, start_col, quarter, axis=1)
    own = lax.all_gather(mine, "grp", axis=0, tiled=True)
    pair = [(i, i ^ 1) for i in range(parts)]

    def device(x, z, k):
        return ((x % side) * side + (z % side)) * 2 + k

    moves = []
    for dx, dz in ((-1, 0), (1, 0), (0, -1), (0, 1)):
        moves.append(
            [
                (device(x, z, k), device(x + dx, z + dz, k))
                for x in range(side)
                for z in range(side)
                for k in range(2)
            ]
        )
    rows_b = own.shape[0] // 4
    from_partner = lax.ppermute(own, "tile", pair)
    received = []
    for b, perm in enumerate(moves):
        received.append(lax.ppermute(own[b * rows_b : (b + 1) * rows_b], "tile", perm))
    valid = recv_ids < per_dest
    row_t = recv_ids // nvt
    col_t = recv_ids % nvt
    col_q = jnp.minimum(col_t // qt, nq - 1)
    unused = ROWT_DEV * qt

    def answer_part(panel_q, q):
        qbase = jnp.where(q == nq - 1, base[nq - 1] // edge, q * qt)
        idx = jnp.where(valid & (col_q == q), row_t * qt + col_t - qbase, unused)
        out = jnp.dot(dense, panel_q, preferred_element_type=jnp.float32).astype(jnp.bfloat16)
        return take_rows(idx, rows_to_tiles(out, edge))

    answer = answer_part(own, mine_q)
    answer = answer + answer_part(from_partner, 2 * colour + 1 - core)
    from_x = jnp.concatenate(received, axis=0)
    from_partner_x = lax.ppermute(from_x, "tile", pair)
    answer = answer + answer_part(from_x, 2 * (1 - colour) + core)
    answer = answer + answer_part(from_partner_x, 2 * (1 - colour) + 1 - core)
    returned = lax.all_to_all(answer, "tile", split_axis=0, concat_axis=0, tiled=True)
    onehot_back = (position[None, :] == jnp.arange(parts * capacity)[:, None]).astype(returned.dtype)
    result_t = jnp.dot(returned.T, onehot_back, preferred_element_type=jnp.float32).astype(returned.dtype)
    return result_t.T.reshape(count, edge, edge)


def solution(mesh):
    in_specs = (
        P(("grp", "tile"), None, None),
        P(("grp", "tile")),
        P(("grp", "tile")),
        P("grp", None),
    )
    out_specs = P(("grp", "tile"), None, None)
    return jax.shard_map(layer, mesh=mesh, in_specs=in_specs, out_specs=out_specs, check_vma=False)
```

```python
import jax
import jax.numpy as jnp
from jax import lax
from jax.sharding import PartitionSpec as P
from jax.experimental import pallas as pl
from jax.experimental.pallas import tpu as pltpu

ROWT_DEV = 8
PLANE = 4


def pick_rows(index, count, data):
    onehot = (index[None, :] == jnp.arange(count)[:, None]).astype(data.dtype)
    return jnp.dot(onehot, data, preferred_element_type=jnp.float32).astype(data.dtype)


def take_rows(index, data):
    onehot = (index[:, None] == jnp.arange(data.shape[0])[None, :]).astype(data.dtype)
    return jnp.dot(onehot, data, preferred_element_type=jnp.float32).astype(data.dtype)


def tiles_to_rows(tiles, row_tiles, edge):
    col_tiles = tiles.shape[0] // row_tiles

    def kernel(x_ref, o_ref):
        for r in range(row_tiles):
            x = x_ref[r * col_tiles : (r + 1) * col_tiles, :]
            x = jnp.swapaxes(x.reshape(col_tiles, edge, edge), 0, 1)
            o_ref[r * edge : (r + 1) * edge, :] = x.reshape(edge, col_tiles * edge)

    nbytes = tiles.size * tiles.dtype.itemsize
    return pl.pallas_call(
        kernel,
        out_shape=jax.ShapeDtypeStruct((row_tiles * edge, col_tiles * edge), tiles.dtype),
        in_specs=[pl.BlockSpec(memory_space=pltpu.VMEM)],
        out_specs=pl.BlockSpec(memory_space=pltpu.VMEM),
        cost_estimate=pl.CostEstimate(flops=0, transcendentals=0, bytes_accessed=2 * nbytes),
    )(tiles)


def rows_to_tiles(rows, edge):
    row_tiles = rows.shape[0] // edge
    col_tiles = rows.shape[1] // edge

    def kernel(x_ref, o_ref):
        for r in range(row_tiles):
            x = x_ref[r * edge : (r + 1) * edge, :]
            x = jnp.swapaxes(x.reshape(edge, col_tiles, edge), 0, 1)
            o_ref[r * col_tiles : (r + 1) * col_tiles, :] = x.reshape(col_tiles, edge * edge)

    nbytes = rows.size * rows.dtype.itemsize
    return pl.pallas_call(
        kernel,
        out_shape=jax.ShapeDtypeStruct((row_tiles * col_tiles, edge * edge), rows.dtype),
        in_specs=[pl.BlockSpec(memory_space=pltpu.VMEM)],
        out_specs=pl.BlockSpec(memory_space=pltpu.VMEM),
        cost_estimate=pl.CostEstimate(flops=0, transcendentals=0, bytes_accessed=2 * nbytes),
    )(rows)


def layer(amp_tiles, amp_row, amp_col, cycle_panel):
    parts = lax.axis_size("tile")
    count = amp_tiles.shape[0]
    capacity = count // parts
    edge = amp_tiles.shape[1]
    width = cycle_panel.shape[1]
    nvt = width // edge
    per_dest = ROWT_DEV * nvt
    group_rows = ROWT_DEV * parts
    first = lax.axis_index("grp") * group_rows
    local_row = amp_row - first
    live = local_row < group_rows
    target = jnp.where(live, local_row // ROWT_DEV, parts)
    onehot = (target[:, None] == jnp.arange(parts)[None, :]).astype(jnp.int32)
    rank = jnp.sum(jnp.cumsum(onehot, axis=0) * onehot, axis=1) - 1
    position = jnp.where(live, target * capacity + rank, parts * capacity)
    block_id = local_row % ROWT_DEV * nvt + amp_col
    flat = amp_tiles.reshape(count, edge * edge)
    send_tiles = pick_rows(position, parts * capacity, flat)
    send_ids = (
        jnp.full((parts * capacity,), per_dest, jnp.int32).at[position].set(block_id, mode="drop")
    )
    recv_tiles, recv_ids = (
        lax.all_to_all(send_tiles, "tile", split_axis=0, concat_axis=0, tiled=True),
        lax.all_to_all(send_ids, "tile", split_axis=0, concat_axis=0, tiled=True),
    )
    dense = tiles_to_rows(pick_rows(recv_ids, per_dest, recv_tiles), ROWT_DEV, edge)
    tile = lax.axis_index("tile")
    core = tile % 2
    chip = tile // 2
    side = PLANE
    cx = chip // side
    cz = chip % side
    colour = (cx + cz) % 2
    quarter = 1024
    nq = 4
    qt = quarter // edge
    base = [min(q * quarter, width - quarter) for q in range(nq)]
    mine_q = 2 * colour + core
    start_col = jnp.where(mine_q == nq - 1, base[nq - 1], mine_q * quarter)
    mine = lax.dynamic_slice_in_dim(cycle_panel, start_col, quarter, axis=1)
    own = lax.all_gather(mine, "grp", axis=0, tiled=True)
    pair = [(i, i ^ 1) for i in range(parts)]

    def device(x, z, k):
        return ((x % side) * side + (z % side)) * 2 + k

    moves = []
    for dx, dz in ((-1, 0), (1, 0), (0, -1), (0, 1)):
        moves.append(
            [
                (device(x, z, k), device(x + dx, z + dz, k))
                for x in range(side)
                for z in range(side)
                for k in range(2)
            ]
        )
    step_rows = 1024
    cuts = [(b * step_rows, min((b + 1) * step_rows, own.shape[0])) for b in range(4)]
    from_partner = lax.ppermute(own, "tile", pair)
    received = []
    for (lo, hi), perm in zip(cuts, moves):
        received.append(lax.ppermute(own[lo:hi], "tile", perm))
    received_partner = [lax.ppermute(piece, "tile", pair) for piece in received]
    valid = recv_ids < per_dest
    row_t = recv_ids // nvt
    col_t = recv_ids % nvt
    col_q = jnp.minimum(col_t // qt, nq - 1)

    def product(panel_q):
        out = jnp.dot(dense, panel_q, preferred_element_type=jnp.float32)
        return rows_to_tiles(out.astype(jnp.bfloat16), edge)

    def product_cut(pieces):
        out = None
        for (lo, hi), piece in zip(cuts, pieces):
            part = jnp.dot(dense[:, lo:hi], piece, preferred_element_type=jnp.float32)
            out = part if out is None else out + part
        return rows_to_tiles(out.astype(jnp.bfloat16), edge)

    blocks_own = product(own)
    blocks_partner = product(from_partner)
    blocks_x = product_cut(received)
    blocks_px = product_cut(received_partner)
    held = [mine_q, 2 * colour + 1 - core, 2 * (1 - colour) + core, 2 * (1 - colour) + 1 - core]
    slot = jnp.zeros_like(col_q)
    for i, q in enumerate(held):
        slot = jnp.where(col_q == q, i, slot)
    qbase = jnp.where(col_q == nq - 1, base[nq - 1] // edge, col_q * qt)
    per_q = ROWT_DEV * qt
    idx = jnp.where(valid, slot * per_q + row_t * qt + col_t - qbase, nq * per_q)
    answer = take_rows(idx, jnp.concatenate([blocks_own, blocks_partner, blocks_x, blocks_px], axis=0))
    returned = lax.all_to_all(answer, "tile", split_axis=0, concat_axis=0, tiled=True)
    onehot_back = (position[None, :] == jnp.arange(parts * capacity)[:, None]).astype(returned.dtype)
    result_t = jnp.dot(returned.T, onehot_back, preferred_element_type=jnp.float32).astype(returned.dtype)
    return result_t.T.reshape(count, edge, edge)


def solution(mesh):
    in_specs = (
        P(("grp", "tile"), None, None),
        P(("grp", "tile")),
        P(("grp", "tile")),
        P("grp", None),
    )
    out_specs = P(("grp", "tile"), None, None)
    return jax.shard_map(layer, mesh=mesh, in_specs=in_specs, out_specs=out_specs, check_vma=False)
```

```python
import jax
import jax.numpy as jnp
from jax import lax
from jax.sharding import PartitionSpec as P
from jax.experimental import pallas as pl
from jax.experimental.pallas import tpu as pltpu

ROWT_DEV = 8
PLANE = 4


def pick_rows(index, count, data):
    onehot = (index[None, :] == jnp.arange(count)[:, None]).astype(data.dtype)
    return jnp.dot(onehot, data, preferred_element_type=jnp.float32).astype(data.dtype)


def take_rows(index, data):
    onehot = (index[:, None] == jnp.arange(data.shape[0])[None, :]).astype(data.dtype)
    return jnp.dot(onehot, data, preferred_element_type=jnp.float32).astype(data.dtype)


def tiles_to_rows(tiles, row_tiles, edge):
    col_tiles = tiles.shape[0] // row_tiles

    def kernel(x_ref, o_ref):
        for r in range(row_tiles):
            x = x_ref[r * col_tiles : (r + 1) * col_tiles, :]
            x = jnp.swapaxes(x.reshape(col_tiles, edge, edge), 0, 1)
            o_ref[r * edge : (r + 1) * edge, :] = x.reshape(edge, col_tiles * edge)

    nbytes = tiles.size * tiles.dtype.itemsize
    return pl.pallas_call(
        kernel,
        out_shape=jax.ShapeDtypeStruct((row_tiles * edge, col_tiles * edge), tiles.dtype),
        in_specs=[pl.BlockSpec(memory_space=pltpu.VMEM)],
        out_specs=pl.BlockSpec(memory_space=pltpu.VMEM),
        cost_estimate=pl.CostEstimate(flops=0, transcendentals=0, bytes_accessed=2 * nbytes),
    )(tiles)


def rows_to_tiles(rows, edge):
    row_tiles = rows.shape[0] // edge
    col_tiles = rows.shape[1] // edge

    def kernel(x_ref, o_ref):
        for r in range(row_tiles):
            x = x_ref[r * edge : (r + 1) * edge, :]
            x = jnp.swapaxes(x.reshape(edge, col_tiles, edge), 0, 1)
            o_ref[r * col_tiles : (r + 1) * col_tiles, :] = x.reshape(col_tiles, edge * edge)

    nbytes = rows.size * rows.dtype.itemsize
    return pl.pallas_call(
        kernel,
        out_shape=jax.ShapeDtypeStruct((row_tiles * col_tiles, edge * edge), rows.dtype),
        in_specs=[pl.BlockSpec(memory_space=pltpu.VMEM)],
        out_specs=pl.BlockSpec(memory_space=pltpu.VMEM),
        cost_estimate=pl.CostEstimate(flops=0, transcendentals=0, bytes_accessed=2 * nbytes),
    )(rows)


def scatter_back(returned, onehot):
    def kernel(r_ref, s_ref, o_ref):
        o_ref[...] = lax.dot_general(
            r_ref[...], s_ref[...], (((0,), (0,)), ((), ())), preferred_element_type=jnp.float32
        ).astype(o_ref.dtype)

    rows, feats = returned.shape
    slots = onehot.shape[1]
    return pl.pallas_call(
        kernel,
        out_shape=jax.ShapeDtypeStruct((feats, slots), returned.dtype),
        in_specs=[pl.BlockSpec(memory_space=pltpu.VMEM)] * 2,
        out_specs=pl.BlockSpec(memory_space=pltpu.VMEM),
        cost_estimate=pl.CostEstimate(
            flops=2 * rows * feats * slots, transcendentals=0, bytes_accessed=2 * (2 * rows * feats + rows * slots)
        ),
    )(returned, onehot)


def layer(amp_tiles, amp_row, amp_col, cycle_panel):
    parts = lax.axis_size("tile")
    count = amp_tiles.shape[0]
    capacity = count // parts
    edge = amp_tiles.shape[1]
    width = cycle_panel.shape[1]
    nvt = width // edge
    per_dest = ROWT_DEV * nvt
    group_rows = ROWT_DEV * parts
    first = lax.axis_index("grp") * group_rows
    local_row = amp_row - first
    live = local_row < group_rows
    target = jnp.where(live, local_row // ROWT_DEV, parts)
    onehot = (target[:, None] == jnp.arange(parts)[None, :]).astype(jnp.int32)
    rank = jnp.sum(jnp.cumsum(onehot, axis=0) * onehot, axis=1) - 1
    position = jnp.where(live, target * capacity + rank, parts * capacity)
    block_id = local_row % ROWT_DEV * nvt + amp_col
    flat = amp_tiles.reshape(count, edge * edge)
    send_tiles = pick_rows(position, parts * capacity, flat)
    send_ids = (
        jnp.full((parts * capacity,), per_dest, jnp.int32).at[position].set(block_id, mode="drop")
    )
    recv_tiles, recv_ids = (
        lax.all_to_all(send_tiles, "tile", split_axis=0, concat_axis=0, tiled=True),
        lax.all_to_all(send_ids, "tile", split_axis=0, concat_axis=0, tiled=True),
    )
    dense = tiles_to_rows(pick_rows(recv_ids, per_dest, recv_tiles), ROWT_DEV, edge)
    tile = lax.axis_index("tile")
    core = tile % 2
    chip = tile // 2
    side = PLANE
    cx = chip // side
    cz = chip % side
    colour = (cx + cz) % 2
    quarter = 1024
    nq = 4
    qt = quarter // edge
    base = [min(q * quarter, width - quarter) for q in range(nq)]
    mine_q = 2 * colour + core
    start_col = jnp.where(mine_q == nq - 1, base[nq - 1], mine_q * quarter)
    mine = lax.dynamic_slice_in_dim(cycle_panel, start_col, quarter, axis=1)
    own = lax.all_gather(mine, "grp", axis=0, tiled=True)
    pair = [(i, i ^ 1) for i in range(parts)]

    def device(x, z, k):
        return ((x % side) * side + (z % side)) * 2 + k

    moves = []
    for dx, dz in ((-1, 0), (1, 0), (0, -1), (0, 1)):
        moves.append(
            [
                (device(x, z, k), device(x + dx, z + dz, k))
                for x in range(side)
                for z in range(side)
                for k in range(2)
            ]
        )
    step_rows = 1024
    cuts = [(b * step_rows, min((b + 1) * step_rows, own.shape[0])) for b in range(4)]
    from_partner = lax.ppermute(own, "tile", pair)
    received = []
    for (lo, hi), perm in zip(cuts, moves):
        received.append(lax.ppermute(own[lo:hi], "tile", perm))
    received_partner = [lax.ppermute(piece, "tile", pair) for piece in received]
    valid = recv_ids < per_dest
    row_t = recv_ids // nvt
    col_t = recv_ids % nvt
    col_q = jnp.minimum(col_t // qt, nq - 1)

    def product(panel_q):
        out = jnp.dot(dense, panel_q, preferred_element_type=jnp.float32)
        return rows_to_tiles(out.astype(jnp.bfloat16), edge)

    def product_cut(pieces):
        out = None
        for (lo, hi), piece in zip(cuts, pieces):
            part = jnp.dot(dense[:, lo:hi], piece, preferred_element_type=jnp.float32)
            out = part if out is None else out + part
        return rows_to_tiles(out.astype(jnp.bfloat16), edge)

    blocks_own = product(own)
    blocks_partner = product(from_partner)
    blocks_x = product_cut(received)
    blocks_px = product_cut(received_partner)
    held = [mine_q, 2 * colour + 1 - core, 2 * (1 - colour) + core, 2 * (1 - colour) + 1 - core]
    slot = jnp.zeros_like(col_q)
    for i, q in enumerate(held):
        slot = jnp.where(col_q == q, i, slot)
    qbase = jnp.where(col_q == nq - 1, base[nq - 1] // edge, col_q * qt)
    per_q = ROWT_DEV * qt
    idx = jnp.where(valid, slot * per_q + row_t * qt + col_t - qbase, nq * per_q)
    answer = take_rows(idx, jnp.concatenate([blocks_own, blocks_partner, blocks_x, blocks_px], axis=0))
    returned = lax.all_to_all(answer, "tile", split_axis=0, concat_axis=0, tiled=True)
    onehot_back = (position[None, :] == jnp.arange(parts * capacity)[:, None]).astype(returned.dtype)
    result_t = scatter_back(returned, onehot_back)
    return result_t.T.reshape(count, edge, edge)


def solution(mesh):
    in_specs = (
        P(("grp", "tile"), None, None),
        P(("grp", "tile")),
        P(("grp", "tile")),
        P("grp", None),
    )
    out_specs = P(("grp", "tile"), None, None)
    return jax.shard_map(layer, mesh=mesh, in_specs=in_specs, out_specs=out_specs, check_vma=False)
```

```python
import jax
import jax.numpy as jnp
from jax import lax
from jax.sharding import PartitionSpec as P
from jax.experimental import pallas as pl
from jax.experimental.pallas import tpu as pltpu

ROWT_DEV = 8
PLANE = 4


def pick_rows(index, count, data):
    onehot = (index[None, :] == jnp.arange(count)[:, None]).astype(data.dtype)
    return jnp.dot(onehot, data, preferred_element_type=jnp.float32).astype(data.dtype)


def take_rows(index, data):
    onehot = (index[:, None] == jnp.arange(data.shape[0])[None, :]).astype(data.dtype)
    return jnp.dot(onehot, data, preferred_element_type=jnp.float32).astype(data.dtype)


def tiles_to_rows(tiles, row_tiles, edge):
    col_tiles = tiles.shape[0] // row_tiles

    def kernel(x_ref, o_ref):
        for r in range(row_tiles):
            x = x_ref[r * col_tiles : (r + 1) * col_tiles, :]
            x = jnp.swapaxes(x.reshape(col_tiles, edge, edge), 0, 1)
            o_ref[r * edge : (r + 1) * edge, :] = x.reshape(edge, col_tiles * edge)

    nbytes = tiles.size * tiles.dtype.itemsize
    return pl.pallas_call(
        kernel,
        out_shape=jax.ShapeDtypeStruct((row_tiles * edge, col_tiles * edge), tiles.dtype),
        in_specs=[pl.BlockSpec(memory_space=pltpu.VMEM)],
        out_specs=pl.BlockSpec(memory_space=pltpu.VMEM),
        cost_estimate=pl.CostEstimate(flops=0, transcendentals=0, bytes_accessed=2 * nbytes),
    )(tiles)


def rows_to_tiles(rows, edge):
    row_tiles = rows.shape[0] // edge
    col_tiles = rows.shape[1] // edge

    def kernel(x_ref, o_ref):
        for r in range(row_tiles):
            x = x_ref[r * edge : (r + 1) * edge, :]
            x = jnp.swapaxes(x.reshape(edge, col_tiles, edge), 0, 1)
            o_ref[r * col_tiles : (r + 1) * col_tiles, :] = x.reshape(col_tiles, edge * edge)

    nbytes = rows.size * rows.dtype.itemsize
    return pl.pallas_call(
        kernel,
        out_shape=jax.ShapeDtypeStruct((row_tiles * col_tiles, edge * edge), rows.dtype),
        in_specs=[pl.BlockSpec(memory_space=pltpu.VMEM)],
        out_specs=pl.BlockSpec(memory_space=pltpu.VMEM),
        cost_estimate=pl.CostEstimate(flops=0, transcendentals=0, bytes_accessed=2 * nbytes),
    )(rows)


def scatter_back(returned, onehot):
    def kernel(r_ref, s_ref, o_ref):
        o_ref[...] = lax.dot_general(
            r_ref[...], s_ref[...], (((0,), (0,)), ((), ())), preferred_element_type=jnp.float32
        ).astype(o_ref.dtype)

    rows, feats = returned.shape
    slots = onehot.shape[1]
    return pl.pallas_call(
        kernel,
        out_shape=jax.ShapeDtypeStruct((feats, slots), returned.dtype),
        in_specs=[pl.BlockSpec(memory_space=pltpu.VMEM)] * 2,
        out_specs=pl.BlockSpec(memory_space=pltpu.VMEM),
        cost_estimate=pl.CostEstimate(
            flops=2 * rows * feats * slots, transcendentals=0, bytes_accessed=2 * (2 * rows * feats + rows * slots)
        ),
    )(returned, onehot)


def layer(amp_tiles, amp_row, amp_col, cycle_panel):
    parts = lax.axis_size("tile")
    count = amp_tiles.shape[0]
    capacity = count // parts
    edge = amp_tiles.shape[1]
    width = cycle_panel.shape[1]
    nvt = width // edge
    per_dest = ROWT_DEV * nvt
    group_rows = ROWT_DEV * parts
    first = lax.axis_index("grp") * group_rows
    local_row = amp_row - first
    live = local_row < group_rows
    target = jnp.where(live, local_row // ROWT_DEV, parts)
    onehot = (target[:, None] == jnp.arange(parts)[None, :]).astype(jnp.int32)
    rank = jnp.sum(jnp.cumsum(onehot, axis=0) * onehot, axis=1) - 1
    position = jnp.where(live, target * capacity + rank, parts * capacity)
    block_id = local_row % ROWT_DEV * nvt + amp_col
    flat = amp_tiles.reshape(count, edge * edge)
    send_tiles = pick_rows(position, parts * capacity, flat)
    send_ids = (
        jnp.full((parts * capacity,), per_dest, jnp.int32).at[position].set(block_id, mode="drop")
    )
    hi = (send_ids // 32).astype(jnp.bfloat16).reshape(parts, capacity)
    lo = (send_ids % 32).astype(jnp.bfloat16).reshape(parts, capacity)
    pad = jnp.zeros((parts, edge * edge - 2 * capacity), jnp.bfloat16)
    id_rows = jnp.concatenate([hi, lo, pad], axis=1)
    payload = jnp.concatenate(
        [send_tiles.reshape(parts, capacity, edge * edge), id_rows[:, None, :]], axis=1
    )
    arrived = lax.all_to_all(payload, "tile", split_axis=0, concat_axis=0, tiled=True)
    recv_tiles = arrived[:, :capacity].reshape(parts * capacity, edge * edge)
    got = arrived[:, capacity, : 2 * capacity].astype(jnp.int32)
    recv_ids = (got[:, :capacity] * 32 + got[:, capacity:]).reshape(parts * capacity)
    dense = tiles_to_rows(pick_rows(recv_ids, per_dest, recv_tiles), ROWT_DEV, edge)
    tile = lax.axis_index("tile")
    core = tile % 2
    chip = tile // 2
    side = PLANE
    cx = chip // side
    cz = chip % side
    colour = (cx + cz) % 2
    quarter = 1024
    nq = 4
    qt = quarter // edge
    base = [min(q * quarter, width - quarter) for q in range(nq)]
    mine_q = 2 * colour + core
    start_col = jnp.where(mine_q == nq - 1, base[nq - 1], mine_q * quarter)
    mine = lax.dynamic_slice_in_dim(cycle_panel, start_col, quarter, axis=1)
    own = lax.all_gather(mine, "grp", axis=0, tiled=True)
    pair = [(i, i ^ 1) for i in range(parts)]

    def device(x, z, k):
        return ((x % side) * side + (z % side)) * 2 + k

    moves = []
    for dx, dz in ((-1, 0), (1, 0), (0, -1), (0, 1)):
        moves.append(
            [
                (device(x, z, k), device(x + dx, z + dz, k))
                for x in range(side)
                for z in range(side)
                for k in range(2)
            ]
        )
    step_rows = 1024
    cuts = [(b * step_rows, min((b + 1) * step_rows, own.shape[0])) for b in range(4)]
    from_partner = lax.ppermute(own, "tile", pair)
    received = []
    for (lo, hi), perm in zip(cuts, moves):
        received.append(lax.ppermute(own[lo:hi], "tile", perm))
    received_partner = [lax.ppermute(piece, "tile", pair) for piece in received]
    valid = recv_ids < per_dest
    row_t = recv_ids // nvt
    col_t = recv_ids % nvt
    col_q = jnp.minimum(col_t // qt, nq - 1)

    def product(panel_q):
        out = jnp.dot(dense, panel_q, preferred_element_type=jnp.float32)
        return rows_to_tiles(out.astype(jnp.bfloat16), edge)

    def product_cut(pieces):
        out = None
        for (lo, hi), piece in zip(cuts, pieces):
            part = jnp.dot(dense[:, lo:hi], piece, preferred_element_type=jnp.float32)
            out = part if out is None else out + part
        return rows_to_tiles(out.astype(jnp.bfloat16), edge)

    blocks_own = product(own)
    blocks_partner = product(from_partner)
    blocks_x = product_cut(received)
    blocks_px = product_cut(received_partner)
    held = [mine_q, 2 * colour + 1 - core, 2 * (1 - colour) + core, 2 * (1 - colour) + 1 - core]
    slot = jnp.zeros_like(col_q)
    for i, q in enumerate(held):
        slot = jnp.where(col_q == q, i, slot)
    qbase = jnp.where(col_q == nq - 1, base[nq - 1] // edge, col_q * qt)
    per_q = ROWT_DEV * qt
    idx = jnp.where(valid, slot * per_q + row_t * qt + col_t - qbase, nq * per_q)
    answer = take_rows(idx, jnp.concatenate([blocks_own, blocks_partner, blocks_x, blocks_px], axis=0))
    returned = lax.all_to_all(answer, "tile", split_axis=0, concat_axis=0, tiled=True)
    onehot_back = (position[None, :] == jnp.arange(parts * capacity)[:, None]).astype(returned.dtype)
    result_t = scatter_back(returned, onehot_back)
    return result_t.T.reshape(count, edge, edge)


def solution(mesh):
    in_specs = (
        P(("grp", "tile"), None, None),
        P(("grp", "tile")),
        P(("grp", "tile")),
        P("grp", None),
    )
    out_specs = P(("grp", "tile"), None, None)
    return jax.shard_map(layer, mesh=mesh, in_specs=in_specs, out_specs=out_specs, check_vma=False)
```

```python
import jax
import jax.numpy as jnp
from jax import lax
from jax.sharding import PartitionSpec as P
from jax.experimental import pallas as pl
from jax.experimental.pallas import tpu as pltpu

ROWT_DEV = 8
PLANE = 4


def pick_rows(index, count, data):
    onehot = (index[None, :] == jnp.arange(count)[:, None]).astype(data.dtype)
    return jnp.dot(onehot, data, preferred_element_type=jnp.float32).astype(data.dtype)


def take_rows(index, data):
    onehot = (index[:, None] == jnp.arange(data.shape[0])[None, :]).astype(data.dtype)
    return jnp.dot(onehot, data, preferred_element_type=jnp.float32).astype(data.dtype)


def tiles_to_rows(tiles, row_tiles, edge):
    col_tiles = tiles.shape[0] // row_tiles

    def kernel(x_ref, o_ref):
        for r in range(row_tiles):
            x = x_ref[r * col_tiles : (r + 1) * col_tiles, :]
            x = jnp.swapaxes(x.reshape(col_tiles, edge, edge), 0, 1)
            o_ref[r * edge : (r + 1) * edge, :] = x.reshape(edge, col_tiles * edge)

    nbytes = tiles.size * tiles.dtype.itemsize
    return pl.pallas_call(
        kernel,
        out_shape=jax.ShapeDtypeStruct((row_tiles * edge, col_tiles * edge), tiles.dtype),
        in_specs=[pl.BlockSpec(memory_space=pltpu.VMEM)],
        out_specs=pl.BlockSpec(memory_space=pltpu.VMEM),
        cost_estimate=pl.CostEstimate(flops=0, transcendentals=0, bytes_accessed=2 * nbytes),
    )(tiles)


def rows_to_tiles(rows, edge):
    row_tiles = rows.shape[0] // edge
    col_tiles = rows.shape[1] // edge

    def kernel(x_ref, o_ref):
        for r in range(row_tiles):
            x = x_ref[r * edge : (r + 1) * edge, :]
            x = jnp.swapaxes(x.reshape(edge, col_tiles, edge), 0, 1)
            o_ref[r * col_tiles : (r + 1) * col_tiles, :] = x.reshape(col_tiles, edge * edge)

    nbytes = rows.size * rows.dtype.itemsize
    return pl.pallas_call(
        kernel,
        out_shape=jax.ShapeDtypeStruct((row_tiles * col_tiles, edge * edge), rows.dtype),
        in_specs=[pl.BlockSpec(memory_space=pltpu.VMEM)],
        out_specs=pl.BlockSpec(memory_space=pltpu.VMEM),
        cost_estimate=pl.CostEstimate(flops=0, transcendentals=0, bytes_accessed=2 * nbytes),
    )(rows)


def scatter_back(returned, onehot):
    def kernel(r_ref, s_ref, o_ref):
        o_ref[...] = lax.dot_general(
            r_ref[...], s_ref[...], (((0,), (0,)), ((), ())), preferred_element_type=jnp.float32
        ).astype(o_ref.dtype)

    rows, feats = returned.shape
    slots = onehot.shape[1]
    return pl.pallas_call(
        kernel,
        out_shape=jax.ShapeDtypeStruct((feats, slots), returned.dtype),
        in_specs=[pl.BlockSpec(memory_space=pltpu.VMEM)] * 2,
        out_specs=pl.BlockSpec(memory_space=pltpu.VMEM),
        cost_estimate=pl.CostEstimate(
            flops=2 * rows * feats * slots, transcendentals=0, bytes_accessed=2 * (2 * rows * feats + rows * slots)
        ),
    )(returned, onehot)


def layer(amp_tiles, amp_row, amp_col, cycle_panel):
    parts = lax.axis_size("tile")
    count = amp_tiles.shape[0]
    capacity = count // parts
    edge = amp_tiles.shape[1]
    width = cycle_panel.shape[1]
    nvt = width // edge
    per_dest = ROWT_DEV * nvt
    group_rows = ROWT_DEV * parts
    first = lax.axis_index("grp") * group_rows
    local_row = amp_row - first
    live = local_row < group_rows
    target = jnp.where(live, local_row // ROWT_DEV, parts)
    onehot = (target[:, None] == jnp.arange(parts)[None, :]).astype(jnp.int32)
    rank = jnp.sum(jnp.cumsum(onehot, axis=0) * onehot, axis=1) - 1
    position = jnp.where(live, target * capacity + rank, parts * capacity)
    block_id = local_row % ROWT_DEV * nvt + amp_col
    flat = amp_tiles.reshape(count, edge * edge)
    send_tiles = pick_rows(position, parts * capacity, flat)
    send_ids = (
        jnp.full((parts * capacity,), per_dest, jnp.int32).at[position].set(block_id, mode="drop")
    )
    recv_tiles = lax.all_to_all(send_tiles, "tile", split_axis=0, concat_axis=0, tiled=True)
    after = lax.optimization_barrier((recv_tiles, send_ids))[1]
    recv_ids = lax.all_to_all(after, "tile", split_axis=0, concat_axis=0, tiled=True)
    dense = tiles_to_rows(pick_rows(recv_ids, per_dest, recv_tiles), ROWT_DEV, edge)
    tile = lax.axis_index("tile")
    core = tile % 2
    chip = tile // 2
    side = PLANE
    cx = chip // side
    cz = chip % side
    colour = (cx + cz) % 2
    quarter = 1024
    nq = 4
    qt = quarter // edge
    base = [min(q * quarter, width - quarter) for q in range(nq)]
    mine_q = 2 * colour + core
    start_col = jnp.where(mine_q == nq - 1, base[nq - 1], mine_q * quarter)
    mine = lax.dynamic_slice_in_dim(cycle_panel, start_col, quarter, axis=1)
    own = lax.all_gather(mine, "grp", axis=0, tiled=True)
    pair = [(i, i ^ 1) for i in range(parts)]

    def device(x, z, k):
        return ((x % side) * side + (z % side)) * 2 + k

    moves = []
    for dx, dz in ((-1, 0), (1, 0), (0, -1), (0, 1)):
        moves.append(
            [
                (device(x, z, k), device(x + dx, z + dz, k))
                for x in range(side)
                for z in range(side)
                for k in range(2)
            ]
        )
    step_rows = 1024
    cuts = [(b * step_rows, min((b + 1) * step_rows, own.shape[0])) for b in range(4)]
    from_partner = lax.ppermute(own, "tile", pair)
    received = []
    for (lo, hi), perm in zip(cuts, moves):
        received.append(lax.ppermute(own[lo:hi], "tile", perm))
    received_partner = [lax.ppermute(piece, "tile", pair) for piece in received]
    valid = recv_ids < per_dest
    row_t = recv_ids // nvt
    col_t = recv_ids % nvt
    col_q = jnp.minimum(col_t // qt, nq - 1)

    def product(panel_q):
        out = jnp.dot(dense, panel_q, preferred_element_type=jnp.float32)
        return rows_to_tiles(out.astype(jnp.bfloat16), edge)

    def product_cut(pieces):
        out = None
        for (lo, hi), piece in zip(cuts, pieces):
            part = jnp.dot(dense[:, lo:hi], piece, preferred_element_type=jnp.float32)
            out = part if out is None else out + part
        return rows_to_tiles(out.astype(jnp.bfloat16), edge)

    blocks_own = product(own)
    blocks_partner = product(from_partner)
    blocks_x = product_cut(received)
    blocks_px = product_cut(received_partner)
    held = [mine_q, 2 * colour + 1 - core, 2 * (1 - colour) + core, 2 * (1 - colour) + 1 - core]
    slot = jnp.zeros_like(col_q)
    for i, q in enumerate(held):
        slot = jnp.where(col_q == q, i, slot)
    qbase = jnp.where(col_q == nq - 1, base[nq - 1] // edge, col_q * qt)
    per_q = ROWT_DEV * qt
    idx = jnp.where(valid, slot * per_q + row_t * qt + col_t - qbase, nq * per_q)
    answer = take_rows(idx, jnp.concatenate([blocks_own, blocks_partner, blocks_x, blocks_px], axis=0))
    returned = lax.all_to_all(answer, "tile", split_axis=0, concat_axis=0, tiled=True)
    onehot_back = (position[None, :] == jnp.arange(parts * capacity)[:, None]).astype(returned.dtype)
    result_t = scatter_back(returned, onehot_back)
    return result_t.T.reshape(count, edge, edge)


def solution(mesh):
    in_specs = (
        P(("grp", "tile"), None, None),
        P(("grp", "tile")),
        P(("grp", "tile")),
        P("grp", None),
    )
    out_specs = P(("grp", "tile"), None, None)
    return jax.shard_map(layer, mesh=mesh, in_specs=in_specs, out_specs=out_specs, check_vma=False)
```

```python
import jax
import jax.numpy as jnp
from jax import lax
from jax.sharding import PartitionSpec as P
from jax.experimental import pallas as pl
from jax.experimental.pallas import tpu as pltpu

ROWT_DEV = 8
PLANE = 4


def pick_rows(index, count, data):
    onehot = (index[None, :] == jnp.arange(count)[:, None]).astype(data.dtype)
    return jnp.dot(onehot, data, preferred_element_type=jnp.float32).astype(data.dtype)


def take_rows(index, data):
    onehot = (index[:, None] == jnp.arange(data.shape[0])[None, :]).astype(data.dtype)
    return jnp.dot(onehot, data, preferred_element_type=jnp.float32).astype(data.dtype)


def tiles_to_rows(tiles, row_tiles, edge, picker):
    col_tiles = picker.shape[0] // row_tiles

    def kernel(t_ref, p_ref, o_ref, x_ref):
        x_ref[...] = jnp.dot(p_ref[...], t_ref[...], preferred_element_type=jnp.float32).astype(x_ref.dtype)
        for r in range(row_tiles):
            x = x_ref[r * col_tiles : (r + 1) * col_tiles, :]
            x = jnp.swapaxes(x.reshape(col_tiles, edge, edge), 0, 1)
            o_ref[r * edge : (r + 1) * edge, :] = x.reshape(edge, col_tiles * edge)

    nbytes = tiles.size * tiles.dtype.itemsize
    return pl.pallas_call(
        kernel,
        out_shape=jax.ShapeDtypeStruct((row_tiles * edge, col_tiles * edge), tiles.dtype),
        in_specs=[pl.BlockSpec(memory_space=pltpu.VMEM)] * 2,
        out_specs=pl.BlockSpec(memory_space=pltpu.VMEM),
        scratch_shapes=[pltpu.VMEM((picker.shape[0], tiles.shape[1]), tiles.dtype)],
        cost_estimate=pl.CostEstimate(
            flops=2 * picker.shape[0] * tiles.shape[0] * tiles.shape[1],
            transcendentals=0,
            bytes_accessed=2 * nbytes + picker.size * picker.dtype.itemsize,
        ),
    )(tiles, picker)


def rows_to_tiles(rows, edge):
    row_tiles = rows.shape[0] // edge
    col_tiles = rows.shape[1] // edge

    def kernel(x_ref, o_ref):
        for r in range(row_tiles):
            x = x_ref[r * edge : (r + 1) * edge, :]
            x = jnp.swapaxes(x.reshape(edge, col_tiles, edge), 0, 1)
            o_ref[r * col_tiles : (r + 1) * col_tiles, :] = x.reshape(col_tiles, edge * edge)

    nbytes = rows.size * rows.dtype.itemsize
    return pl.pallas_call(
        kernel,
        out_shape=jax.ShapeDtypeStruct((row_tiles * col_tiles, edge * edge), rows.dtype),
        in_specs=[pl.BlockSpec(memory_space=pltpu.VMEM)],
        out_specs=pl.BlockSpec(memory_space=pltpu.VMEM),
        cost_estimate=pl.CostEstimate(flops=0, transcendentals=0, bytes_accessed=2 * nbytes),
    )(rows)


def scatter_back(returned, onehot):
    def kernel(r_ref, s_ref, o_ref):
        o_ref[...] = lax.dot_general(
            r_ref[...], s_ref[...], (((0,), (0,)), ((), ())), preferred_element_type=jnp.float32
        ).astype(o_ref.dtype)

    rows, feats = returned.shape
    slots = onehot.shape[1]
    return pl.pallas_call(
        kernel,
        out_shape=jax.ShapeDtypeStruct((feats, slots), returned.dtype),
        in_specs=[pl.BlockSpec(memory_space=pltpu.VMEM)] * 2,
        out_specs=pl.BlockSpec(memory_space=pltpu.VMEM),
        cost_estimate=pl.CostEstimate(
            flops=2 * rows * feats * slots, transcendentals=0, bytes_accessed=2 * (2 * rows * feats + rows * slots)
        ),
    )(returned, onehot)


def layer(amp_tiles, amp_row, amp_col, cycle_panel):
    parts = lax.axis_size("tile")
    count = amp_tiles.shape[0]
    capacity = count // parts
    edge = amp_tiles.shape[1]
    width = cycle_panel.shape[1]
    nvt = width // edge
    per_dest = ROWT_DEV * nvt
    group_rows = ROWT_DEV * parts
    first = lax.axis_index("grp") * group_rows
    local_row = amp_row - first
    live = local_row < group_rows
    target = jnp.where(live, local_row // ROWT_DEV, parts)
    onehot = (target[:, None] == jnp.arange(parts)[None, :]).astype(jnp.int32)
    rank = jnp.sum(jnp.cumsum(onehot, axis=0) * onehot, axis=1) - 1
    position = jnp.where(live, target * capacity + rank, parts * capacity)
    block_id = local_row % ROWT_DEV * nvt + amp_col
    flat = amp_tiles.reshape(count, edge * edge)
    send_tiles = pick_rows(position, parts * capacity, flat)
    send_ids = (
        jnp.full((parts * capacity,), per_dest, jnp.int32).at[position].set(block_id, mode="drop")
    )
    recv_tiles, recv_ids = (
        lax.all_to_all(send_tiles, "tile", split_axis=0, concat_axis=0, tiled=True),
        lax.all_to_all(send_ids, "tile", split_axis=0, concat_axis=0, tiled=True),
    )
    picker = (recv_ids[None, :] == jnp.arange(per_dest)[:, None]).astype(recv_tiles.dtype)
    dense = tiles_to_rows(recv_tiles, ROWT_DEV, edge, picker)
    tile = lax.axis_index("tile")
    core = tile % 2
    chip = tile // 2
    side = PLANE
    cx = chip // side
    cz = chip % side
    colour = (cx + cz) % 2
    quarter = 1024
    nq = 4
    qt = quarter // edge
    base = [min(q * quarter, width - quarter) for q in range(nq)]
    mine_q = 2 * colour + core
    start_col = jnp.where(mine_q == nq - 1, base[nq - 1], mine_q * quarter)
    mine = lax.dynamic_slice_in_dim(cycle_panel, start_col, quarter, axis=1)
    own = lax.all_gather(mine, "grp", axis=0, tiled=True)
    pair = [(i, i ^ 1) for i in range(parts)]

    def device(x, z, k):
        return ((x % side) * side + (z % side)) * 2 + k

    moves = []
    for dx, dz in ((-1, 0), (1, 0), (0, -1), (0, 1)):
        moves.append(
            [
                (device(x, z, k), device(x + dx, z + dz, k))
                for x in range(side)
                for z in range(side)
                for k in range(2)
            ]
        )
    step_rows = 1024
    cuts = [(b * step_rows, min((b + 1) * step_rows, own.shape[0])) for b in range(4)]
    from_partner = lax.ppermute(own, "tile", pair)
    received = []
    for (lo, hi), perm in zip(cuts, moves):
        received.append(lax.ppermute(own[lo:hi], "tile", perm))
    received_partner = [lax.ppermute(piece, "tile", pair) for piece in received]
    valid = recv_ids < per_dest
    row_t = recv_ids // nvt
    col_t = recv_ids % nvt
    col_q = jnp.minimum(col_t // qt, nq - 1)

    def product(panel_q):
        out = jnp.dot(dense, panel_q, preferred_element_type=jnp.float32)
        return rows_to_tiles(out.astype(jnp.bfloat16), edge)

    def product_cut(pieces):
        out = None
        for (lo, hi), piece in zip(cuts, pieces):
            part = jnp.dot(dense[:, lo:hi], piece, preferred_element_type=jnp.float32)
            out = part if out is None else out + part
        return rows_to_tiles(out.astype(jnp.bfloat16), edge)

    blocks_own = product(own)
    blocks_partner = product(from_partner)
    blocks_x = product_cut(received)
    blocks_px = product_cut(received_partner)
    held = [mine_q, 2 * colour + 1 - core, 2 * (1 - colour) + core, 2 * (1 - colour) + 1 - core]
    slot = jnp.zeros_like(col_q)
    for i, q in enumerate(held):
        slot = jnp.where(col_q == q, i, slot)
    qbase = jnp.where(col_q == nq - 1, base[nq - 1] // edge, col_q * qt)
    per_q = ROWT_DEV * qt
    idx = jnp.where(valid, slot * per_q + row_t * qt + col_t - qbase, nq * per_q)
    answer = take_rows(idx, jnp.concatenate([blocks_own, blocks_partner, blocks_x, blocks_px], axis=0))
    returned = lax.all_to_all(answer, "tile", split_axis=0, concat_axis=0, tiled=True)
    onehot_back = (position[None, :] == jnp.arange(parts * capacity)[:, None]).astype(returned.dtype)
    result_t = scatter_back(returned, onehot_back)
    return result_t.T.reshape(count, edge, edge)


def solution(mesh):
    in_specs = (
        P(("grp", "tile"), None, None),
        P(("grp", "tile")),
        P(("grp", "tile")),
        P("grp", None),
    )
    out_specs = P(("grp", "tile"), None, None)
    return jax.shard_map(layer, mesh=mesh, in_specs=in_specs, out_specs=out_specs, check_vma=False)
```

```python
import jax
import jax.numpy as jnp
from jax import lax
from jax.sharding import PartitionSpec as P
from jax.experimental import pallas as pl
from jax.experimental.pallas import tpu as pltpu

ROWT_DEV = 8
PLANE = 4


def pick_rows(index, count, data):
    onehot = (index[None, :] == jnp.arange(count)[:, None]).astype(data.dtype)
    return jnp.dot(onehot, data, preferred_element_type=jnp.float32).astype(data.dtype)


def tiles_to_rows(tiles, row_tiles, edge, picker):
    col_tiles = picker.shape[0] // row_tiles

    def kernel(t_ref, p_ref, o_ref, x_ref):
        x_ref[...] = jnp.dot(p_ref[...], t_ref[...], preferred_element_type=jnp.float32).astype(x_ref.dtype)
        for r in range(row_tiles):
            x = x_ref[r * col_tiles : (r + 1) * col_tiles, :]
            x = jnp.swapaxes(x.reshape(col_tiles, edge, edge), 0, 1)
            o_ref[r * edge : (r + 1) * edge, :] = x.reshape(edge, col_tiles * edge)

    nbytes = tiles.size * tiles.dtype.itemsize
    return pl.pallas_call(
        kernel,
        out_shape=jax.ShapeDtypeStruct((row_tiles * edge, col_tiles * edge), tiles.dtype),
        in_specs=[pl.BlockSpec(memory_space=pltpu.VMEM)] * 2,
        out_specs=pl.BlockSpec(memory_space=pltpu.VMEM),
        scratch_shapes=[pltpu.VMEM((picker.shape[0], tiles.shape[1]), tiles.dtype)],
        cost_estimate=pl.CostEstimate(
            flops=2 * picker.shape[0] * tiles.shape[0] * tiles.shape[1],
            transcendentals=0,
            bytes_accessed=2 * nbytes + picker.size * picker.dtype.itemsize,
        ),
    )(tiles, picker)


def rows_to_tiles(rows, edge):
    row_tiles = rows.shape[0] // edge
    col_tiles = rows.shape[1] // edge

    def kernel(x_ref, o_ref):
        for r in range(row_tiles):
            x = x_ref[r * edge : (r + 1) * edge, :]
            x = jnp.swapaxes(x.reshape(edge, col_tiles, edge), 0, 1)
            o_ref[r * col_tiles : (r + 1) * col_tiles, :] = x.reshape(col_tiles, edge * edge)

    nbytes = rows.size * rows.dtype.itemsize
    return pl.pallas_call(
        kernel,
        out_shape=jax.ShapeDtypeStruct((row_tiles * col_tiles, edge * edge), rows.dtype),
        in_specs=[pl.BlockSpec(memory_space=pltpu.VMEM)],
        out_specs=pl.BlockSpec(memory_space=pltpu.VMEM),
        cost_estimate=pl.CostEstimate(flops=0, transcendentals=0, bytes_accessed=2 * nbytes),
    )(rows)


def scatter_back(returned, onehot):
    def kernel(r_ref, s_ref, o_ref):
        o_ref[...] = lax.dot_general(
            r_ref[...], s_ref[...], (((0,), (0,)), ((), ())), preferred_element_type=jnp.float32
        ).astype(o_ref.dtype)

    rows, feats = returned.shape
    slots = onehot.shape[1]
    return pl.pallas_call(
        kernel,
        out_shape=jax.ShapeDtypeStruct((feats, slots), returned.dtype),
        in_specs=[pl.BlockSpec(memory_space=pltpu.VMEM)] * 2,
        out_specs=pl.BlockSpec(memory_space=pltpu.VMEM),
        cost_estimate=pl.CostEstimate(
            flops=2 * rows * feats * slots, transcendentals=0, bytes_accessed=2 * (2 * rows * feats + rows * slots)
        ),
    )(returned, onehot)


def gather_answer(blocks, last_rows, picker, edge):
    row_tiles = last_rows.shape[0] // edge
    col_tiles = last_rows.shape[1] // edge
    per = row_tiles * col_tiles

    def kernel(b0_ref, b1_ref, b2_ref, r_ref, p_ref, o_ref, t_ref):
        for r in range(row_tiles):
            x = r_ref[r * edge : (r + 1) * edge, :]
            x = jnp.swapaxes(x.reshape(edge, col_tiles, edge), 0, 1)
            t_ref[r * col_tiles : (r + 1) * col_tiles, :] = x.reshape(col_tiles, edge * edge)
        acc = None
        for i, ref in enumerate((b0_ref, b1_ref, b2_ref, t_ref)):
            part = jnp.dot(p_ref[:, i * per : (i + 1) * per], ref[...], preferred_element_type=jnp.float32)
            acc = part if acc is None else acc + part
        o_ref[...] = acc.astype(o_ref.dtype)

    slots = picker.shape[0]
    feats = edge * edge
    return pl.pallas_call(
        kernel,
        out_shape=jax.ShapeDtypeStruct((slots, feats), last_rows.dtype),
        in_specs=[pl.BlockSpec(memory_space=pltpu.VMEM)] * 5,
        out_specs=pl.BlockSpec(memory_space=pltpu.VMEM),
        scratch_shapes=[pltpu.VMEM((per, feats), last_rows.dtype)],
        cost_estimate=pl.CostEstimate(
            flops=2 * slots * 4 * per * feats, transcendentals=0, bytes_accessed=2 * (5 * per * feats + slots * feats)
        ),
    )(*blocks, last_rows, picker)


def layer(amp_tiles, amp_row, amp_col, cycle_panel):
    parts = lax.axis_size("tile")
    count = amp_tiles.shape[0]
    capacity = count // parts
    edge = amp_tiles.shape[1]
    width = cycle_panel.shape[1]
    nvt = width // edge
    per_dest = ROWT_DEV * nvt
    group_rows = ROWT_DEV * parts
    first = lax.axis_index("grp") * group_rows
    local_row = amp_row - first
    live = local_row < group_rows
    target = jnp.where(live, local_row // ROWT_DEV, parts)
    onehot = (target[:, None] == jnp.arange(parts)[None, :]).astype(jnp.int32)
    rank = jnp.sum(jnp.cumsum(onehot, axis=0) * onehot, axis=1) - 1
    position = jnp.where(live, target * capacity + rank, parts * capacity)
    block_id = local_row % ROWT_DEV * nvt + amp_col
    flat = amp_tiles.reshape(count, edge * edge)
    send_tiles = pick_rows(position, parts * capacity, flat)
    send_ids = (
        jnp.full((parts * capacity,), per_dest, jnp.int32).at[position].set(block_id, mode="drop")
    )
    recv_tiles, recv_ids = (
        lax.all_to_all(send_tiles, "tile", split_axis=0, concat_axis=0, tiled=True),
        lax.all_to_all(send_ids, "tile", split_axis=0, concat_axis=0, tiled=True),
    )
    picker = (recv_ids[None, :] == jnp.arange(per_dest)[:, None]).astype(recv_tiles.dtype)
    dense = tiles_to_rows(recv_tiles, ROWT_DEV, edge, picker)
    tile = lax.axis_index("tile")
    core = tile % 2
    chip = tile // 2
    side = PLANE
    cx = chip // side
    cz = chip % side
    colour = (cx + cz) % 2
    quarter = 1024
    nq = 4
    qt = quarter // edge
    base = [min(q * quarter, width - quarter) for q in range(nq)]
    mine_q = 2 * colour + core
    start_col = jnp.where(mine_q == nq - 1, base[nq - 1], mine_q * quarter)
    mine = lax.dynamic_slice_in_dim(cycle_panel, start_col, quarter, axis=1)
    own = lax.all_gather(mine, "grp", axis=0, tiled=True)
    pair = [(i, i ^ 1) for i in range(parts)]

    def device(x, z, k):
        return ((x % side) * side + (z % side)) * 2 + k

    moves = []
    for dx, dz in ((-1, 0), (1, 0), (0, -1), (0, 1)):
        moves.append(
            [
                (device(x, z, k), device(x + dx, z + dz, k))
                for x in range(side)
                for z in range(side)
                for k in range(2)
            ]
        )
    step_rows = 1024
    cuts = [(b * step_rows, min((b + 1) * step_rows, own.shape[0])) for b in range(4)]
    from_partner = lax.ppermute(own, "tile", pair)
    received = []
    for (lo, hi), perm in zip(cuts, moves):
        received.append(lax.ppermute(own[lo:hi], "tile", perm))
    received_partner = [lax.ppermute(piece, "tile", pair) for piece in received]
    valid = recv_ids < per_dest
    row_t = recv_ids // nvt
    col_t = recv_ids % nvt
    col_q = jnp.minimum(col_t // qt, nq - 1)

    def product(panel_q):
        out = jnp.dot(dense, panel_q, preferred_element_type=jnp.float32)
        return rows_to_tiles(out.astype(jnp.bfloat16), edge)

    def product_cut(pieces):
        out = None
        for (lo, hi), piece in zip(cuts, pieces):
            part = jnp.dot(dense[:, lo:hi], piece, preferred_element_type=jnp.float32)
            out = part if out is None else out + part
        return rows_to_tiles(out.astype(jnp.bfloat16), edge)

    blocks_own = product(own)
    blocks_partner = product(from_partner)
    blocks_x = product_cut(received)
    out_px = None
    for (lo, hi), piece in zip(cuts, received_partner):
        part = jnp.dot(dense[:, lo:hi], piece, preferred_element_type=jnp.float32)
        out_px = part if out_px is None else out_px + part
    out_px = out_px.astype(jnp.bfloat16)
    held = [mine_q, 2 * colour + 1 - core, 2 * (1 - colour) + core, 2 * (1 - colour) + 1 - core]
    slot = jnp.zeros_like(col_q)
    for i, q in enumerate(held):
        slot = jnp.where(col_q == q, i, slot)
    qbase = jnp.where(col_q == nq - 1, base[nq - 1] // edge, col_q * qt)
    per_q = ROWT_DEV * qt
    idx = jnp.where(valid, slot * per_q + row_t * qt + col_t - qbase, nq * per_q)
    picker = (idx[:, None] == jnp.arange(nq * per_q)[None, :]).astype(jnp.bfloat16)
    answer = gather_answer((blocks_own, blocks_partner, blocks_x), out_px, picker, edge)
    returned = lax.all_to_all(answer, "tile", split_axis=0, concat_axis=0, tiled=True)
    onehot_back = (position[None, :] == jnp.arange(parts * capacity)[:, None]).astype(returned.dtype)
    result_t = scatter_back(returned, onehot_back)
    return result_t.T.reshape(count, edge, edge)


def solution(mesh):
    in_specs = (
        P(("grp", "tile"), None, None),
        P(("grp", "tile")),
        P(("grp", "tile")),
        P("grp", None),
    )
    out_specs = P(("grp", "tile"), None, None)
    return jax.shard_map(layer, mesh=mesh, in_specs=in_specs, out_specs=out_specs, check_vma=False)
```
